128 devices in a mesh: row: 16 (over z, y), col: 8 (over x, core).
Axes of the slice: x: 4, y: 4, z: 4, core: 2. Of those that a mesh axis runs over, the one named last changes fastest.
Arguments:
- child_inverse: float32 [16384, 8192], P('row', 'col'), may hold values from -0.0625 to 0.0625
- child_border: float32 [32768, 8192], P('row', 'col'), may hold values from -0.0625 to 0.0625
- child_sep_rhs: float32 [16384, 128], P('row'), may hold values from -6 to 6
- child_border_rhs: float32 [32768, 128], P(('row', 'col')), may hold values from -6 to 6
- child_map: int32 [32768], P(('row', 'col')), may hold values from 0 to 24575, as said below
- parent_inverse: float32 [8192, 8192], P('row', 'col'), may hold values from -0.0625 to 0.0625
- parent_border: float32 [16384, 8192], P('row', 'col'), may hold values from -0.0625 to 0.0625
- parent_sep_rhs: float32 [8192, 128], P(('row', 'col')), may hold values from -6 to 6
- parent_border_rhs: float32 [16384, 128], P(('row', 'col')), may hold values from -6 to 6
Outputs:
- child_solution: float32 [8192, 256], P('col', 'row')
- parent_solution: float32 [8192, 128], P('col')
- parent_contribution: float32 [16384, 128], P(('row', 'col'))
The draws below stay inside these ranges and needn't reach their ends.
Inputs may be any that keep to these rules, and one draw needn't show every extreme that they name: `child_map`: within one child (entries c * 16384 to (c + 1) * 16384 - 1) all entries are distinct; each child names every separator row 0 to 8191 and, of each owner's 128 border rows, exactly half. The owner of parent row p is p // 64 if p < 8192, else (p - 8192) // 128; every owner is named by exactly 128 entries of each child. Of the 256 entries of one device (aligned blocks), at most 4 name the same owner, and this is reached in every draw.
All inputs are finite; a program needn't handle non-finite values.
Results may differ from the reference program's by a relative error of at most 0.00012.
Values sent between devices are 32-bit elements; how exact they have to be, the bound alone decides.
No kernel may reach another device: no remote copies, remote signals or barrier semaphores. Data moves between devices by JAX's collectives and lax.ppermute only.
A program may use at most 64 MiB of HBM per device.

```python
import jax
import jax.numpy as jnp
from jax import lax

SC = 8192
SP = 8192
BP = 16384
NRHS = 128
BC = 16384
ROWS_SRC = 256
SEP_DEV = 64
BORD_DEV = 128
MEAN_SENT = 2
CAP = 4


def sign_pair(key, length):
    rank_of = jax.random.permutation(key, length).astype(jnp.int32)
    eighth = length // 8
    first_sign = jnp.where(rank_of < 2 * eighth, 1, jnp.where(rank_of < 4 * eighth, -1, 0))
    plus_second = (rank_of < eighth) | (rank_of >= 4 * eighth) & (rank_of < 5 * eighth)
    minus_second = (rank_of >= 2 * eighth) & (rank_of < 3 * eighth) | (rank_of >= 5 * eighth) & (rank_of < 6 * eighth)
    second_sign = jnp.where(plus_second, 1, jnp.where(minus_second, -1, 0))
    return (first_sign.astype(jnp.int32), second_sign.astype(jnp.int32))


def child_targets(key, owners, sources, quota_rows):
    subkeys = jax.random.split(key, 5)
    source_one, source_two = sign_pair(subkeys[0], sources)
    owner_one, owner_two = sign_pair(subkeys[1], owners)
    counts = MEAN_SENT + source_one[:, None] * owner_one[None, :] + source_two[:, None] * owner_two[None, :]
    offsets = jnp.cumsum(counts, axis=0) - counts
    owner_ids = jnp.arange(owners, dtype=jnp.int32)[:, None]
    border_pool = jnp.tile(jnp.arange(BORD_DEV, dtype=jnp.int32)[None, :], (owners, 1))
    border_pick = jax.random.permutation(subkeys[2], border_pool, axis=1, independent=True)[:, :BORD_DEV // 2]
    sep_part = owner_ids * SEP_DEV + jnp.arange(SEP_DEV, dtype=jnp.int32)[None, :]
    border_part = SP + owner_ids * BORD_DEV + border_pick
    targets = jnp.concatenate([sep_part, border_part], axis=1)
    targets = jax.random.permutation(subkeys[3], targets, axis=1, independent=True)
    slot_ids = jnp.arange(CAP, dtype=jnp.int32)
    position = jnp.clip(offsets[:, :, None] + slot_ids[None, None, :], 0, quota_rows - 1)
    is_live = slot_ids[None, None, :] < counts[:, :, None]
    picked = targets[jnp.arange(owners, dtype=jnp.int32)[None, :, None], position]
    picked_flat = picked.reshape(sources, owners * CAP)
    dead_key = 1 - is_live.reshape(sources, owners * CAP).astype(jnp.int32)
    live_first = jnp.argsort(dead_key, axis=1, stable=True)[:, :ROWS_SRC]
    row_targets = jnp.take_along_axis(picked_flat, live_first, axis=1)
    row_targets = jax.random.permutation(subkeys[4], row_targets, axis=1, independent=True)
    return row_targets.reshape(-1).astype(jnp.int32)


def draw_child_map(key, part):
    owners = SP // SEP_DEV
    sources = BC // ROWS_SRC
    quota_rows = SEP_DEV + BORD_DEV // 2
    halves = [child_targets(jax.random.fold_in(key, 11 + member), owners, sources, quota_rows) for member in range(2)]
    return jnp.concatenate(halves).astype(jnp.int32)


def steps_of(key, shape, shards, low, high):
    level = 1.0
    for dim, parts in shards:
        draws = jax.random.uniform(jax.random.fold_in(jax.random.fold_in(key, 6), dim), (parts,), jnp.float32, low / len(shards), high / len(shards))
        level = level * jnp.repeat(jnp.exp(draws), shape[dim] // parts).reshape((-1,) + (1,) * (len(shape) - 1 - dim))
    return level


def centred(rng, dims, width, most, cuts=(), held_as=jnp.bfloat16):
    drawn = width * jax.random.normal(rng, dims, jnp.float32)
    if cuts:
        drawn = drawn * steps_of(rng, dims, cuts, -0.22, 0.18)
    return jnp.clip(drawn, -most, most).astype(held_as)


def setup_inputs(seed: int = 0) -> dict:
    arg_keys = jax.random.split(jax.random.key(seed), 10)
    child_inverse = centred(arg_keys[0], (2 * SC, SC), SC ** -0.5, 0.0625, ((0, 16), (1, 8)), jnp.float32)
    child_border = centred(arg_keys[1], (2 * BC, SC), SC ** -0.5, 0.0625, ((0, 16), (1, 8)), jnp.float32)
    child_sep_rhs = centred(arg_keys[2], (2 * SC, NRHS), 1.0, 6.0, ((0, 16),), jnp.float32)
    child_border_rhs = centred(arg_keys[3], (2 * BC, NRHS), 1.0, 6.0, ((0, 128),), jnp.float32)
    child_map = draw_child_map(jax.random.fold_in(arg_keys[9], 71), 0)
    parent_inverse = centred(arg_keys[5], (SP, SP), SP ** -0.5, 0.0625, ((0, 16), (1, 8)), jnp.float32)
    parent_border = centred(arg_keys[6], (BP, SP), SP ** -0.5, 0.0625, ((0, 16), (1, 8)), jnp.float32)
    parent_sep_rhs = centred(arg_keys[7], (SP, NRHS), 1.0, 6.0, ((0, 128),), jnp.float32)
    parent_border_rhs = centred(arg_keys[8], (BP, NRHS), 1.0, 6.0, ((0, 128),), jnp.float32)
    return {"child_inverse": child_inverse, "child_border": child_border, "child_sep_rhs": child_sep_rhs, "child_border_rhs": child_border_rhs, "child_map": child_map, "parent_inverse": parent_inverse, "parent_border": parent_border, "parent_sep_rhs": parent_sep_rhs, "parent_border_rhs": parent_border_rhs}


def reference(child_inverse, child_border, child_sep_rhs, child_border_rhs, child_map, parent_inverse, parent_border, parent_sep_rhs, parent_border_rhs):
    highest = lax.Precision.HIGHEST
    contract_rows = (((0,), (0,)), ((), ()))
    assembled = jnp.concatenate([parent_sep_rhs, parent_border_rhs], axis=0)
    solved_list = []
    for member in range(2):
        inverse_t = child_inverse[member * SC:(member + 1) * SC]
        sep_values = child_sep_rhs[member * SC:(member + 1) * SC]
        solved_block = lax.dot_general(inverse_t, sep_values, contract_rows, precision=highest, preferred_element_type=jnp.float32)
        solved_list.append(solved_block)
        border_block = child_border[member * BC:(member + 1) * BC]
        update = child_border_rhs[member * BC:(member + 1) * BC] - jnp.dot(border_block, solved_block, precision=highest, preferred_element_type=jnp.float32)
        target_rows = child_map[member * BC:(member + 1) * BC].astype(jnp.int32)
        assembled = assembled.at[target_rows].add(update)
    parent_solution = lax.dot_general(parent_inverse, assembled[:SP], contract_rows, precision=highest, preferred_element_type=jnp.float32)
    parent_contribution = assembled[SP:] - jnp.dot(parent_border, parent_solution, precision=highest, preferred_element_type=jnp.float32)
    return jnp.concatenate(solved_list, axis=1), parent_solution, parent_contribution
```

```python
import jax
import jax.numpy as jnp
from jax import lax
from jax.sharding import Mesh
from jax.sharding import PartitionSpec as P

SP = 8192
ROW = ("h", "r8")
ALL = ("h", "r8", "col")


def reduce_scatter(x, axis, n):
    got = lax.all_to_all(x.reshape(n, x.shape[0] // n, x.shape[1]), axis, 0, 0, tiled=False)
    return got.sum(axis=0)


def gather(x, axis, n):
    got = lax.all_to_all(jnp.broadcast_to(x[None], (n,) + x.shape), axis, 0, 0, tiled=False)
    return got.reshape(n * x.shape[0], x.shape[1])


def local(
    child_inverse,
    child_border,
    child_sep_rhs,
    child_border_rhs,
    child_map,
    parent_inverse,
    parent_border,
    parent_sep_rhs,
    parent_border_rhs,
):
    highest = lax.Precision.HIGHEST
    contract_rows = (((0,), (0,)), ((), ()))
    half_rows = lax.axis_size("r8")
    rows_axis = lax.axis_size("h") * half_rows
    cols_axis = lax.axis_size("col")
    within = lax.axis_index("r8")
    partial_term = lax.dot_general(
        child_inverse,
        child_sep_rhs,
        contract_rows,
        precision=highest,
        preferred_element_type=jnp.float32,
    )
    width_rhs = partial_term.shape[1]
    solved = gather(reduce_scatter(partial_term, "r8", half_rows), "r8", half_rows)
    share = width_rhs // half_rows
    child_part = lax.dynamic_slice_in_dim(solved, within * share, share, axis=1)
    carried = reduce_scatter(
        jnp.dot(child_border, solved, precision=highest, preferred_element_type=jnp.float32),
        "col",
        cols_axis,
    )
    outgoing = child_border_rhs - carried
    devices_all = rows_axis * cols_axis
    sep_dev = parent_sep_rhs.shape[0]
    bord_dev = parent_border_rhs.shape[0]
    rows_src = child_map.shape[0]
    capacity = rows_src // devices_all + 2
    is_sep = child_map < SP
    owner_id = jnp.where(is_sep, child_map // sep_dev, (child_map - SP) // bord_dev)
    target = jnp.where(is_sep, child_map % sep_dev, sep_dev + (child_map - SP) % bord_dev)
    onehot = (owner_id[:, None] == jnp.arange(devices_all, dtype=jnp.int32)[None, :]).astype(
        jnp.int32
    )
    running = jnp.cumsum(onehot, axis=0)
    placed = owner_id * capacity + jnp.sum(onehot * running, axis=1) - 1
    send_rows = jnp.zeros((devices_all * capacity, width_rhs), jnp.float32).at[placed].set(outgoing)
    send_index = (
        jnp.full((devices_all * capacity,), sep_dev + bord_dev, jnp.int32).at[placed].set(target)
    )
    got_rows = lax.all_to_all(
        send_rows.reshape(devices_all, capacity, width_rhs), ALL, 0, 0, tiled=True
    )
    got_index = lax.all_to_all(send_index.reshape(devices_all, capacity), ALL, 0, 0, tiled=True)
    received = (
        jnp.zeros((sep_dev + bord_dev, width_rhs), jnp.float32)
        .at[got_index.reshape(-1)]
        .add(got_rows.reshape(-1, width_rhs), mode="drop")
    )
    sep_rows = parent_sep_rhs + received[:sep_dev]
    border_rows = parent_border_rhs + received[sep_dev:]
    partial_sep = lax.dot_general(
        parent_inverse,
        gather(sep_rows, "col", cols_axis),
        contract_rows,
        precision=highest,
        preferred_element_type=jnp.float32,
    )
    parent_solution = gather(reduce_scatter(partial_sep, ROW, rows_axis), ROW, rows_axis)
    carried_parent = reduce_scatter(
        jnp.dot(parent_border, parent_solution, precision=highest, preferred_element_type=jnp.float32),
        "col",
        cols_axis,
    )
    parent_contribution = border_rows - carried_parent
    return (child_part, parent_solution, parent_contribution)


def solution(mesh):
    rows, cols = mesh.devices.shape
    split = Mesh(mesh.devices.reshape(2, rows // 2, cols), ("h", "r8", "col"))
    placed = (
        P(ROW, "col"),
        P(ROW, "col"),
        P(ROW, None),
        P(ALL, None),
        P(ALL),
        P(ROW, "col"),
        P(ROW, "col"),
        P(ALL, None),
        P(ALL, None),
    )
    return jax.shard_map(
        local,
        mesh=split,
        in_specs=placed,
        out_specs=(P("col", ROW), P("col", None), P(ALL, None)),
        check_vma=False,
    )
```

```python
import jax
import jax.numpy as jnp
from jax import lax
from jax.sharding import Mesh
from jax.sharding import PartitionSpec as P

SP = 8192
ROW = ("h", "r8")
ALL = ("h", "r8", "col")


def reduce_scatter(x, axis, n):
    got = lax.all_to_all(x.reshape(n, x.shape[0] // n, x.shape[1]), axis, 0, 0, tiled=False)
    return got.sum(axis=0)


def gather(x, axis, n):
    got = lax.all_to_all(jnp.broadcast_to(x[None], (n,) + x.shape), axis, 0, 0, tiled=False)
    return got.reshape(n * x.shape[0], x.shape[1])


def local(
    child_inverse,
    child_border,
    child_sep_rhs,
    child_border_rhs,
    child_map,
    parent_inverse,
    parent_border,
    parent_sep_rhs,
    parent_border_rhs,
):
    highest = lax.Precision.HIGHEST
    contract_rows = (((0,), (0,)), ((), ()))
    half_rows = lax.axis_size("r8")
    rows_axis = lax.axis_size("h") * half_rows
    cols_axis = lax.axis_size("col")
    within = lax.axis_index("r8")
    partial_term = lax.dot_general(
        child_inverse,
        child_sep_rhs,
        contract_rows,
        precision=highest,
        preferred_element_type=jnp.float32,
    )
    width_rhs = partial_term.shape[1]
    solved = gather(reduce_scatter(partial_term, "r8", half_rows), "r8", half_rows)
    share = width_rhs // half_rows
    child_part = lax.dynamic_slice_in_dim(solved, within * share, share, axis=1)
    carried = reduce_scatter(
        jnp.dot(child_border, solved, precision=highest, preferred_element_type=jnp.float32),
        "col",
        cols_axis,
    )
    outgoing = child_border_rhs - carried
    devices_all = rows_axis * cols_axis
    sep_dev = parent_sep_rhs.shape[0]
    bord_dev = parent_border_rhs.shape[0]
    rows_src = child_map.shape[0]
    capacity = rows_src // devices_all + 2
    is_sep = child_map < SP
    owner_id = jnp.where(is_sep, child_map // sep_dev, (child_map - SP) // bord_dev)
    target = jnp.where(is_sep, child_map % sep_dev, sep_dev + (child_map - SP) % bord_dev)
    onehot = (owner_id[:, None] == jnp.arange(devices_all, dtype=jnp.int32)[None, :]).astype(
        jnp.int32
    )
    running = jnp.cumsum(onehot, axis=0)
    placed = owner_id * capacity + jnp.sum(onehot * running, axis=1) - 1
    send_rows = jnp.zeros((devices_all * capacity, width_rhs), jnp.float32).at[placed].set(outgoing)
    send_index = (
        jnp.full((devices_all * capacity,), sep_dev + bord_dev, jnp.int32).at[placed].set(target)
    )
    index_row = jnp.zeros((devices_all, 1, width_rhs), jnp.float32).at[:, 0, :capacity].set(
        send_index.reshape(devices_all, capacity).astype(jnp.float32)
    )
    packed = jnp.concatenate(
        [send_rows.reshape(devices_all, capacity, width_rhs), index_row], axis=1
    )
    got = lax.all_to_all(packed, ALL, 0, 0, tiled=True)
    got_rows = got[:, :capacity]
    got_index = got[:, capacity, :capacity].astype(jnp.int32)
    received = (
        jnp.zeros((sep_dev + bord_dev, width_rhs), jnp.float32)
        .at[got_index.reshape(-1)]
        .add(got_rows.reshape(-1, width_rhs), mode="drop")
    )
    sep_rows = parent_sep_rhs + received[:sep_dev]
    border_rows = parent_border_rhs + received[sep_dev:]
    partial_sep = lax.dot_general(
        parent_inverse,
        gather(sep_rows, "col", cols_axis),
        contract_rows,
        precision=highest,
        preferred_element_type=jnp.float32,
    )
    parent_solution = gather(reduce_scatter(partial_sep, ROW, rows_axis), ROW, rows_axis)
    carried_parent = reduce_scatter(
        jnp.dot(parent_border, parent_solution, precision=highest, preferred_element_type=jnp.float32),
        "col",
        cols_axis,
    )
    parent_contribution = border_rows - carried_parent
    return (child_part, parent_solution, parent_contribution)


def solution(mesh):
    rows, cols = mesh.devices.shape
    split = Mesh(mesh.devices.reshape(2, rows // 2, cols), ("h", "r8", "col"))
    placed = (
        P(ROW, "col"),
        P(ROW, "col"),
        P(ROW, None),
        P(ALL, None),
        P(ALL),
        P(ROW, "col"),
        P(ROW, "col"),
        P(ALL, None),
        P(ALL, None),
    )
    return jax.shard_map(
        local,
        mesh=split,
        in_specs=placed,
        out_specs=(P("col", ROW), P("col", None), P(ALL, None)),
        check_vma=False,
    )
```

```python
import jax
import jax.numpy as jnp
from jax import lax
from jax.sharding import Mesh
from jax.sharding import PartitionSpec as P

SP = 8192
ROW = ("h", "r8")
ALL = ("h", "r8", "col")


def reduce_scatter(x, axis, n):
    got = lax.all_to_all(x.reshape(n, x.shape[0] // n, x.shape[1]), axis, 0, 0, tiled=False)
    return got.sum(axis=0)


def gather(x, axis, n):
    got = lax.all_to_all(jnp.broadcast_to(x[None], (n,) + x.shape), axis, 0, 0, tiled=False)
    return got.reshape(n * x.shape[0], x.shape[1])


def local(
    child_inverse,
    child_border,
    child_sep_rhs,
    child_border_rhs,
    child_map,
    parent_inverse,
    parent_border,
    parent_sep_rhs,
    parent_border_rhs,
):
    highest = lax.Precision.HIGH
    contract_rows = (((0,), (0,)), ((), ()))
    half_rows = lax.axis_size("r8")
    rows_axis = lax.axis_size("h") * half_rows
    cols_axis = lax.axis_size("col")
    within = lax.axis_index("r8")
    partial_term = lax.dot_general(
        child_inverse,
        child_sep_rhs,
        contract_rows,
        precision=highest,
        preferred_element_type=jnp.float32,
    )
    width_rhs = partial_term.shape[1]
    solved = gather(reduce_scatter(partial_term, "r8", half_rows), "r8", half_rows)
    share = width_rhs // half_rows
    child_part = lax.dynamic_slice_in_dim(solved, within * share, share, axis=1)
    carried = reduce_scatter(
        jnp.dot(child_border, solved, precision=highest, preferred_element_type=jnp.float32),
        "col",
        cols_axis,
    )
    outgoing = child_border_rhs - carried
    devices_all = rows_axis * cols_axis
    sep_dev = parent_sep_rhs.shape[0]
    bord_dev = parent_border_rhs.shape[0]
    rows_src = child_map.shape[0]
    capacity = rows_src // devices_all + 2
    is_sep = child_map < SP
    owner_id = jnp.where(is_sep, child_map // sep_dev, (child_map - SP) // bord_dev)
    target = jnp.where(is_sep, child_map % sep_dev, sep_dev + (child_map - SP) % bord_dev)
    onehot = (owner_id[:, None] == jnp.arange(devices_all, dtype=jnp.int32)[None, :]).astype(
        jnp.int32
    )
    running = jnp.cumsum(onehot, axis=0)
    placed = owner_id * capacity + jnp.sum(onehot * running, axis=1) - 1
    send_rows = jnp.zeros((devices_all * capacity, width_rhs), jnp.float32).at[placed].set(outgoing)
    send_index = (
        jnp.full((devices_all * capacity,), sep_dev + bord_dev, jnp.int32).at[placed].set(target)
    )
    index_row = jnp.zeros((devices_all, 1, width_rhs), jnp.float32).at[:, 0, :capacity].set(
        send_index.reshape(devices_all, capacity).astype(jnp.float32)
    )
    packed = jnp.concatenate(
        [send_rows.reshape(devices_all, capacity, width_rhs), index_row], axis=1
    )
    got = lax.all_to_all(packed, ALL, 0, 0, tiled=True)
    got_rows = got[:, :capacity]
    got_index = got[:, capacity, :capacity].astype(jnp.int32)
    received = (
        jnp.zeros((sep_dev + bord_dev, width_rhs), jnp.float32)
        .at[got_index.reshape(-1)]
        .add(got_rows.reshape(-1, width_rhs), mode="drop")
    )
    sep_rows = parent_sep_rhs + received[:sep_dev]
    border_rows = parent_border_rhs + received[sep_dev:]
    partial_sep = lax.dot_general(
        parent_inverse,
        gather(sep_rows, "col", cols_axis),
        contract_rows,
        precision=highest,
        preferred_element_type=jnp.float32,
    )
    parent_solution = gather(reduce_scatter(partial_sep, ROW, rows_axis), ROW, rows_axis)
    carried_parent = reduce_scatter(
        jnp.dot(parent_border, parent_solution, precision=highest, preferred_element_type=jnp.float32),
        "col",
        cols_axis,
    )
    parent_contribution = border_rows - carried_parent
    return (child_part, parent_solution, parent_contribution)


def solution(mesh):
    rows, cols = mesh.devices.shape
    split = Mesh(mesh.devices.reshape(2, rows // 2, cols), ("h", "r8", "col"))
    placed = (
        P(ROW, "col"),
        P(ROW, "col"),
        P(ROW, None),
        P(ALL, None),
        P(ALL),
        P(ROW, "col"),
        P(ROW, "col"),
        P(ALL, None),
        P(ALL, None),
    )
    return jax.shard_map(
        local,
        mesh=split,
        in_specs=placed,
        out_specs=(P("col", ROW), P("col", None), P(ALL, None)),
        check_vma=False,
    )
```

```python
import jax
import jax.numpy as jnp
from jax import lax
from jax.sharding import Mesh
from jax.sharding import PartitionSpec as P

SP = 8192
ROW = ("h", "r8")
ALL = ("h", "r8", "col")


def reduce_scatter(x, axis, n):
    got = lax.all_to_all(x.reshape(n, x.shape[0] // n, x.shape[1]), axis, 0, 0, tiled=False)
    return got.sum(axis=0)


def gather(x, axis, n):
    got = lax.all_to_all(jnp.broadcast_to(x[None], (n,) + x.shape), axis, 0, 0, tiled=False)
    return got.reshape(n * x.shape[0], x.shape[1])


def local(
    child_inverse,
    child_border,
    child_sep_rhs,
    child_border_rhs,
    child_map,
    parent_inverse,
    parent_border,
    parent_sep_rhs,
    parent_border_rhs,
):
    highest = lax.Precision.HIGH
    exact = lax.Precision.HIGHEST
    contract_rows = (((0,), (0,)), ((), ()))
    half_rows = lax.axis_size("r8")
    rows_axis = lax.axis_size("h") * half_rows
    cols_axis = lax.axis_size("col")
    within = lax.axis_index("r8")
    partial_term = lax.dot_general(
        child_inverse,
        child_sep_rhs,
        contract_rows,
        precision=highest,
        preferred_element_type=jnp.float32,
    )
    width_rhs = partial_term.shape[1]
    solved = gather(reduce_scatter(partial_term, "r8", half_rows), "r8", half_rows)
    share = width_rhs // half_rows
    child_part = lax.dynamic_slice_in_dim(solved, within * share, share, axis=1)
    carried = reduce_scatter(
        jnp.dot(child_border, solved, precision=highest, preferred_element_type=jnp.float32),
        "col",
        cols_axis,
    )
    outgoing = child_border_rhs - carried
    devices_all = rows_axis * cols_axis
    sep_dev = parent_sep_rhs.shape[0]
    bord_dev = parent_border_rhs.shape[0]
    rows_src = child_map.shape[0]
    capacity = rows_src // devices_all + 2
    is_sep = child_map < SP
    owner_id = jnp.where(is_sep, child_map // sep_dev, (child_map - SP) // bord_dev)
    target = jnp.where(is_sep, child_map % sep_dev, sep_dev + (child_map - SP) % bord_dev)
    slots = devices_all * capacity
    onehot = (owner_id[:, None] == jnp.arange(devices_all, dtype=jnp.int32)[None, :]).astype(
        jnp.int32
    )
    running = jnp.cumsum(onehot, axis=0)
    placed = owner_id * capacity + jnp.sum(onehot * running, axis=1) - 1
    spread = (jnp.arange(slots, dtype=jnp.int32)[:, None] == placed[None, :]).astype(jnp.float32)
    send_index = (
        jnp.full((slots,), sep_dev + bord_dev, jnp.int32).at[placed].set(target)
    )
    index_row = jnp.zeros((devices_all, 1, width_rhs), jnp.float32).at[:, 0, :capacity].set(
        send_index.reshape(devices_all, capacity).astype(jnp.float32)
    )
    send_rows = jnp.dot(spread, outgoing, precision=exact, preferred_element_type=jnp.float32)
    packed = jnp.concatenate(
        [send_rows.reshape(devices_all, capacity, width_rhs), index_row], axis=1
    )
    got = lax.all_to_all(packed, ALL, 0, 0, tiled=True)
    got_rows = got[:, :capacity].reshape(slots, width_rhs)
    got_index = got[:, capacity, :capacity].astype(jnp.int32).reshape(slots)
    gather_map = (
        jnp.arange(sep_dev + bord_dev, dtype=jnp.int32)[:, None] == got_index[None, :]
    ).astype(jnp.float32)
    received = jnp.dot(gather_map, got_rows, precision=exact, preferred_element_type=jnp.float32)
    sep_rows = parent_sep_rhs + received[:sep_dev]
    border_rows = parent_border_rhs + received[sep_dev:]
    partial_sep = lax.dot_general(
        parent_inverse,
        gather(sep_rows, "col", cols_axis),
        contract_rows,
        precision=highest,
        preferred_element_type=jnp.float32,
    )
    parent_solution = gather(reduce_scatter(partial_sep, ROW, rows_axis), ROW, rows_axis)
    carried_parent = reduce_scatter(
        jnp.dot(parent_border, parent_solution, precision=highest, preferred_element_type=jnp.float32),
        "col",
        cols_axis,
    )
    parent_contribution = border_rows - carried_parent
    return (child_part, parent_solution, parent_contribution)


def solution(mesh):
    rows, cols = mesh.devices.shape
    split = Mesh(mesh.devices.reshape(2, rows // 2, cols), ("h", "r8", "col"))
    placed = (
        P(ROW, "col"),
        P(ROW, "col"),
        P(ROW, None),
        P(ALL, None),
        P(ALL),
        P(ROW, "col"),
        P(ROW, "col"),
        P(ALL, None),
        P(ALL, None),
    )
    return jax.shard_map(
        local,
        mesh=split,
        in_specs=placed,
        out_specs=(P("col", ROW), P("col", None), P(ALL, None)),
        check_vma=False,
    )
```

```python
import jax
import jax.numpy as jnp
from jax import lax
from jax.sharding import Mesh
from jax.sharding import PartitionSpec as P

SP = 8192
ROW = ("h", "r8")
COL = ("x", "k")
ALL = ("h", "r8", "x", "k")


def reduce_scatter(x, axis, n):
    got = lax.all_to_all(x.reshape(n, x.shape[0] // n, x.shape[1]), axis, 0, 0, tiled=False)
    return got.sum(axis=0)


def reduce_scatter_chip(x, chips):
    core = lax.axis_index("k")
    blocks = x.reshape(chips, 2, x.shape[0] // (2 * chips), x.shape[1])
    mine = lax.dynamic_index_in_dim(blocks, core, 1, keepdims=False)
    other = lax.dynamic_index_in_dim(blocks, 1 - core, 1, keepdims=False)
    summed = mine + lax.ppermute(other, "k", [(0, 1), (1, 0)])
    got = lax.all_to_all(summed, "x", 0, 0, tiled=False)
    return got.sum(axis=0)


def gather(x, axis, n):
    got = lax.all_to_all(jnp.broadcast_to(x[None], (n,) + x.shape), axis, 0, 0, tiled=False)
    return got.reshape(n * x.shape[0], x.shape[1])


def local(
    child_inverse,
    child_border,
    child_sep_rhs,
    child_border_rhs,
    child_map,
    parent_inverse,
    parent_border,
    parent_sep_rhs,
    parent_border_rhs,
):
    highest = lax.Precision.HIGH
    exact = lax.Precision.HIGHEST
    contract_rows = (((0,), (0,)), ((), ()))
    half_rows = lax.axis_size("r8")
    rows_axis = lax.axis_size("h") * half_rows
    chips = lax.axis_size("x")
    cols_axis = chips * lax.axis_size("k")
    within = lax.axis_index("r8")
    partial_term = lax.dot_general(
        child_inverse,
        child_sep_rhs,
        contract_rows,
        precision=highest,
        preferred_element_type=jnp.float32,
    )
    width_rhs = partial_term.shape[1]
    solved = gather(reduce_scatter(partial_term, "r8", half_rows), "r8", half_rows)
    share = width_rhs // half_rows
    child_part = lax.dynamic_slice_in_dim(solved, within * share, share, axis=1)
    carried = reduce_scatter_chip(
        jnp.dot(child_border, solved, precision=highest, preferred_element_type=jnp.float32),
        chips,
    )
    outgoing = child_border_rhs - carried
    devices_all = rows_axis * cols_axis
    sep_dev = parent_sep_rhs.shape[0]
    bord_dev = parent_border_rhs.shape[0]
    rows_src = child_map.shape[0]
    capacity = rows_src // devices_all + 2
    is_sep = child_map < SP
    owner_id = jnp.where(is_sep, child_map // sep_dev, (child_map - SP) // bord_dev)
    target = jnp.where(is_sep, child_map % sep_dev, sep_dev + (child_map - SP) % bord_dev)
    slots = devices_all * capacity
    onehot = (owner_id[:, None] == jnp.arange(devices_all, dtype=jnp.int32)[None, :]).astype(
        jnp.int32
    )
    running = jnp.cumsum(onehot, axis=0)
    placed = owner_id * capacity + jnp.sum(onehot * running, axis=1) - 1
    spread = (jnp.arange(slots, dtype=jnp.int32)[:, None] == placed[None, :]).astype(jnp.float32)
    send_index = (
        jnp.full((slots,), sep_dev + bord_dev, jnp.int32).at[placed].set(target)
    )
    index_row = jnp.zeros((devices_all, 1, width_rhs), jnp.float32).at[:, 0, :capacity].set(
        send_index.reshape(devices_all, capacity).astype(jnp.float32)
    )
    send_rows = jnp.dot(spread, outgoing, precision=exact, preferred_element_type=jnp.float32)
    packed = jnp.concatenate(
        [send_rows.reshape(devices_all, capacity, width_rhs), index_row], axis=1
    )
    got = lax.all_to_all(packed, ALL, 0, 0, tiled=True)
    got_rows = got[:, :capacity].reshape(slots, width_rhs)
    got_index = got[:, capacity, :capacity].astype(jnp.int32).reshape(slots)
    gather_map = (
        jnp.arange(sep_dev + bord_dev, dtype=jnp.int32)[:, None] == got_index[None, :]
    ).astype(jnp.float32)
    received = jnp.dot(gather_map, got_rows, precision=exact, preferred_element_type=jnp.float32)
    sep_rows = parent_sep_rhs + received[:sep_dev]
    border_rows = parent_border_rhs + received[sep_dev:]
    partial_sep = lax.dot_general(
        parent_inverse,
        gather(sep_rows, COL, cols_axis),
        contract_rows,
        precision=highest,
        preferred_element_type=jnp.float32,
    )
    parent_solution = gather(reduce_scatter(partial_sep, ROW, rows_axis), ROW, rows_axis)
    carried_parent = reduce_scatter(
        jnp.dot(parent_border, parent_solution, precision=highest, preferred_element_type=jnp.float32),
        COL,
        cols_axis,
    )
    parent_contribution = border_rows - carried_parent
    return (child_part, parent_solution, parent_contribution)


def solution(mesh):
    rows, cols = mesh.devices.shape
    split = Mesh(mesh.devices.reshape(2, rows // 2, cols // 2, 2), ALL)
    placed = (
        P(ROW, COL),
        P(ROW, COL),
        P(ROW, None),
        P(ALL, None),
        P(ALL),
        P(ROW, COL),
        P(ROW, COL),
        P(ALL, None),
        P(ALL, None),
    )
    return jax.shard_map(
        local,
        mesh=split,
        in_specs=placed,
        out_specs=(P(COL, ROW), P(COL, None), P(ALL, None)),
        check_vma=False,
    )
```

```python
import jax
import jax.numpy as jnp
from jax import lax
from jax.sharding import Mesh
from jax.sharding import PartitionSpec as P

SP = 8192
ROW = ("h", "r8")
COL = ("x", "k")
ALL = ("h", "r8", "x", "k")


def reduce_scatter(x, axis, n):
    got = lax.all_to_all(x.reshape(n, x.shape[0] // n, x.shape[1]), axis, 0, 0, tiled=False)
    return got.sum(axis=0)


def reduce_scatter_chip(matrix, vector, chips, precision):
    first = lax.axis_index("k") == 0
    blocks = matrix.reshape(chips, 2, matrix.shape[0] // (2 * chips), matrix.shape[1])
    even, odd = (
        jnp.einsum(
            "xrb,bn->xrn",
            blocks[:, half],
            vector,
            precision=precision,
            preferred_element_type=jnp.float32,
        )
        for half in (0, 1)
    )
    mine = jnp.where(first, even, odd)
    other = jnp.where(first, odd, even)
    summed = mine + lax.ppermute(other, "k", [(0, 1), (1, 0)])
    got = lax.all_to_all(summed, "x", 0, 0, tiled=False)
    return got.sum(axis=0)


def gather(x, axis, n):
    got = lax.all_to_all(jnp.broadcast_to(x[None], (n,) + x.shape), axis, 0, 0, tiled=False)
    return got.reshape(n * x.shape[0], x.shape[1])


def local(
    child_inverse,
    child_border,
    child_sep_rhs,
    child_border_rhs,
    child_map,
    parent_inverse,
    parent_border,
    parent_sep_rhs,
    parent_border_rhs,
):
    highest = lax.Precision.HIGH
    exact = lax.Precision.HIGHEST
    contract_rows = (((0,), (0,)), ((), ()))
    half_rows = lax.axis_size("r8")
    rows_axis = lax.axis_size("h") * half_rows
    chips = lax.axis_size("x")
    cols_axis = chips * lax.axis_size("k")
    within = lax.axis_index("r8")
    partial_term = lax.dot_general(
        child_inverse,
        child_sep_rhs,
        contract_rows,
        precision=highest,
        preferred_element_type=jnp.float32,
    )
    width_rhs = partial_term.shape[1]
    solved = gather(reduce_scatter(partial_term, "r8", half_rows), "r8", half_rows)
    share = width_rhs // half_rows
    child_part = lax.dynamic_slice_in_dim(solved, within * share, share, axis=1)
    carried = reduce_scatter_chip(child_border, solved, chips, highest)
    outgoing = child_border_rhs - carried
    devices_all = rows_axis * cols_axis
    sep_dev = parent_sep_rhs.shape[0]
    bord_dev = parent_border_rhs.shape[0]
    rows_src = child_map.shape[0]
    capacity = rows_src // devices_all + 2
    is_sep = child_map < SP
    owner_id = jnp.where(is_sep, child_map // sep_dev, (child_map - SP) // bord_dev)
    target = jnp.where(is_sep, child_map % sep_dev, sep_dev + (child_map - SP) % bord_dev)
    slots = devices_all * capacity
    onehot = (owner_id[:, None] == jnp.arange(devices_all, dtype=jnp.int32)[None, :]).astype(
        jnp.int32
    )
    running = jnp.cumsum(onehot, axis=0)
    placed = owner_id * capacity + jnp.sum(onehot * running, axis=1) - 1
    spread = (jnp.arange(slots, dtype=jnp.int32)[:, None] == placed[None, :]).astype(jnp.float32)
    send_index = (
        jnp.full((slots,), sep_dev + bord_dev, jnp.int32).at[placed].set(target)
    )
    index_row = jnp.zeros((devices_all, 1, width_rhs), jnp.float32).at[:, 0, :capacity].set(
        send_index.reshape(devices_all, capacity).astype(jnp.float32)
    )
    send_rows = jnp.dot(spread, outgoing, precision=exact, preferred_element_type=jnp.float32)
    packed = jnp.concatenate(
        [send_rows.reshape(devices_all, capacity, width_rhs), index_row], axis=1
    )
    got = lax.all_to_all(packed, ALL, 0, 0, tiled=True)
    got_rows = got[:, :capacity].reshape(slots, width_rhs)
    got_index = got[:, capacity, :capacity].astype(jnp.int32).reshape(slots)
    gather_map = (
        jnp.arange(sep_dev + bord_dev, dtype=jnp.int32)[:, None] == got_index[None, :]
    ).astype(jnp.float32)
    received = jnp.dot(gather_map, got_rows, precision=exact, preferred_element_type=jnp.float32)
    sep_rows = parent_sep_rhs + received[:sep_dev]
    border_rows = parent_border_rhs + received[sep_dev:]
    partial_sep = lax.dot_general(
        parent_inverse,
        gather(sep_rows, COL, cols_axis),
        contract_rows,
        precision=highest,
        preferred_element_type=jnp.float32,
    )
    parent_solution = gather(reduce_scatter(partial_sep, ROW, rows_axis), ROW, rows_axis)
    carried_parent = reduce_scatter(
        jnp.dot(parent_border, parent_solution, precision=highest, preferred_element_type=jnp.float32),
        COL,
        cols_axis,
    )
    parent_contribution = border_rows - carried_parent
    return (child_part, parent_solution, parent_contribution)


def solution(mesh):
    rows, cols = mesh.devices.shape
    split = Mesh(mesh.devices.reshape(2, rows // 2, cols // 2, 2), ALL)
    placed = (
        P(ROW, COL),
        P(ROW, COL),
        P(ROW, None),
        P(ALL, None),
        P(ALL),
        P(ROW, COL),
        P(ROW, COL),
        P(ALL, None),
        P(ALL, None),
    )
    return jax.shard_map(
        local,
        mesh=split,
        in_specs=placed,
        out_specs=(P(COL, ROW), P(COL, None), P(ALL, None)),
        check_vma=False,
    )
```

```python
import jax
import jax.numpy as jnp
from jax import lax
from jax.sharding import Mesh
from jax.sharding import PartitionSpec as P

SP = 8192
ROW = ("h", "r8")
COL = ("x", "k")
ALL = ("h", "r8", "x", "k")


def reduce_scatter(x, axis, n):
    got = lax.all_to_all(x.reshape(n, x.shape[0] // n, x.shape[1]), axis, 0, 0, tiled=False)
    return got.sum(axis=0)


def reduce_scatter_chip(matrix, vector, chips, precision):
    first = lax.axis_index("k") == 0
    blocks = matrix.reshape(chips, 2, matrix.shape[0] // (2 * chips), matrix.shape[1])
    rows = blocks.shape[2]
    even, odd = (
        jnp.dot(
            blocks[:, half].reshape(chips * rows, matrix.shape[1]),
            vector,
            precision=precision,
            preferred_element_type=jnp.float32,
        ).reshape(chips, rows, vector.shape[1])
        for half in (0, 1)
    )
    mine = jnp.where(first, even, odd)
    other = jnp.where(first, odd, even)
    summed = mine + lax.ppermute(other, "k", [(0, 1), (1, 0)])
    got = lax.all_to_all(summed, "x", 0, 0, tiled=False)
    return got.sum(axis=0)


def gather(x, axis, n):
    got = lax.all_to_all(jnp.broadcast_to(x[None], (n,) + x.shape), axis, 0, 0, tiled=False)
    return got.reshape(n * x.shape[0], x.shape[1])


def local(
    child_inverse,
    child_border,
    child_sep_rhs,
    child_border_rhs,
    child_map,
    parent_inverse,
    parent_border,
    parent_sep_rhs,
    parent_border_rhs,
):
    highest = lax.Precision.HIGH
    exact = lax.Precision.HIGHEST
    contract_rows = (((0,), (0,)), ((), ()))
    half_rows = lax.axis_size("r8")
    rows_axis = lax.axis_size("h") * half_rows
    chips = lax.axis_size("x")
    cols_axis = chips * lax.axis_size("k")
    within = lax.axis_index("r8")
    partial_term = lax.dot_general(
        child_inverse,
        child_sep_rhs,
        contract_rows,
        precision=highest,
        preferred_element_type=jnp.float32,
    )
    width_rhs = partial_term.shape[1]
    solved = gather(reduce_scatter(partial_term, "r8", half_rows), "r8", half_rows)
    share = width_rhs // half_rows
    child_part = lax.dynamic_slice_in_dim(solved, within * share, share, axis=1)
    carried = reduce_scatter_chip(child_border, solved, chips, highest)
    outgoing = child_border_rhs - carried
    devices_all = rows_axis * cols_axis
    sep_dev = parent_sep_rhs.shape[0]
    bord_dev = parent_border_rhs.shape[0]
    rows_src = child_map.shape[0]
    capacity = rows_src // devices_all + 2
    is_sep = child_map < SP
    owner_id = jnp.where(is_sep, child_map // sep_dev, (child_map - SP) // bord_dev)
    target = jnp.where(is_sep, child_map % sep_dev, sep_dev + (child_map - SP) % bord_dev)
    slots = devices_all * capacity
    onehot = (owner_id[:, None] == jnp.arange(devices_all, dtype=jnp.int32)[None, :]).astype(
        jnp.int32
    )
    running = jnp.cumsum(onehot, axis=0)
    placed = owner_id * capacity + jnp.sum(onehot * running, axis=1) - 1
    spread = (jnp.arange(slots, dtype=jnp.int32)[:, None] == placed[None, :]).astype(jnp.float32)
    send_index = (
        jnp.full((slots,), sep_dev + bord_dev, jnp.int32).at[placed].set(target)
    )
    index_row = jnp.zeros((devices_all, 1, width_rhs), jnp.float32).at[:, 0, :capacity].set(
        send_index.reshape(devices_all, capacity).astype(jnp.float32)
    )
    send_rows = jnp.dot(spread, outgoing, precision=exact, preferred_element_type=jnp.float32)
    packed = jnp.concatenate(
        [send_rows.reshape(devices_all, capacity, width_rhs), index_row], axis=1
    )
    got = lax.all_to_all(packed, ALL, 0, 0, tiled=True)
    got_rows = got[:, :capacity].reshape(slots, width_rhs)
    got_index = got[:, capacity, :capacity].astype(jnp.int32).reshape(slots)
    gather_map = (
        jnp.arange(sep_dev + bord_dev, dtype=jnp.int32)[:, None] == got_index[None, :]
    ).astype(jnp.float32)
    received = jnp.dot(gather_map, got_rows, precision=exact, preferred_element_type=jnp.float32)
    sep_rows = parent_sep_rhs + received[:sep_dev]
    border_rows = parent_border_rhs + received[sep_dev:]
    partial_sep = lax.dot_general(
        parent_inverse,
        gather(sep_rows, COL, cols_axis),
        contract_rows,
        precision=highest,
        preferred_element_type=jnp.float32,
    )
    parent_solution = gather(reduce_scatter(partial_sep, ROW, rows_axis), ROW, rows_axis)
    carried_parent = reduce_scatter(
        jnp.dot(parent_border, parent_solution, precision=highest, preferred_element_type=jnp.float32),
        COL,
        cols_axis,
    )
    parent_contribution = border_rows - carried_parent
    return (child_part, parent_solution, parent_contribution)


def solution(mesh):
    rows, cols = mesh.devices.shape
    split = Mesh(mesh.devices.reshape(2, rows // 2, cols // 2, 2), ALL)
    placed = (
        P(ROW, COL),
        P(ROW, COL),
        P(ROW, None),
        P(ALL, None),
        P(ALL),
        P(ROW, COL),
        P(ROW, COL),
        P(ALL, None),
        P(ALL, None),
    )
    return jax.shard_map(
        local,
        mesh=split,
        in_specs=placed,
        out_specs=(P(COL, ROW), P(COL, None), P(ALL, None)),
        check_vma=False,
    )
```

```python
import jax
import jax.numpy as jnp
from jax import lax
from jax.sharding import Mesh
from jax.sharding import PartitionSpec as P

SP = 8192
ROW = ("h", "r8")
COL = ("x", "k")
ALL = ("h", "r8", "x", "k")


def reduce_scatter(x, axis, n):
    got = lax.all_to_all(x.reshape(n, x.shape[0] // n, x.shape[1]), axis, 0, 0, tiled=False)
    return got.sum(axis=0)


def reduce_scatter_chip(matrix, vector, chips, precision):
    first = lax.axis_index("k") == 0
    blocks = matrix.reshape(chips, 2, matrix.shape[0] // (2 * chips), matrix.shape[1])
    even, odd = (
        jnp.einsum(
            "xrb,bn->xrn",
            blocks[:, half],
            vector,
            precision=precision,
            preferred_element_type=jnp.float32,
        )
        for half in (0, 1)
    )
    mine = jnp.where(first, even, odd)
    other = jnp.where(first, odd, even)
    summed = mine + lax.ppermute(other, "k", [(0, 1), (1, 0)])
    got = lax.all_to_all(summed, "x", 0, 0, tiled=False)
    return got.sum(axis=0)


def gather_chip(x, chips):
    first = lax.axis_index("k") == 0
    pair = lax.ppermute(x, "k", [(0, 1), (1, 0)])
    both = jnp.concatenate([jnp.where(first, x, pair), jnp.where(first, pair, x)], axis=0)
    return gather(both, "x", chips)


def gather(x, axis, n):
    got = lax.all_to_all(jnp.broadcast_to(x[None], (n,) + x.shape), axis, 0, 0, tiled=False)
    return got.reshape(n * x.shape[0], x.shape[1])


def local(
    child_inverse,
    child_border,
    child_sep_rhs,
    child_border_rhs,
    child_map,
    parent_inverse,
    parent_border,
    parent_sep_rhs,
    parent_border_rhs,
):
    highest = lax.Precision.HIGH
    exact = lax.Precision.HIGHEST
    contract_rows = (((0,), (0,)), ((), ()))
    half_rows = lax.axis_size("r8")
    rows_axis = lax.axis_size("h") * half_rows
    chips = lax.axis_size("x")
    cols_axis = chips * lax.axis_size("k")
    within = lax.axis_index("r8")
    partial_term = lax.dot_general(
        child_inverse,
        child_sep_rhs,
        contract_rows,
        precision=highest,
        preferred_element_type=jnp.float32,
    )
    width_rhs = partial_term.shape[1]
    solved = gather(reduce_scatter(partial_term, "r8", half_rows), "r8", half_rows)
    share = width_rhs // half_rows
    child_part = lax.dynamic_slice_in_dim(solved, within * share, share, axis=1)
    carried = reduce_scatter_chip(child_border, solved, chips, highest)
    outgoing = child_border_rhs - carried
    devices_all = rows_axis * cols_axis
    sep_dev = parent_sep_rhs.shape[0]
    bord_dev = parent_border_rhs.shape[0]
    rows_src = child_map.shape[0]
    capacity = rows_src // devices_all + 2
    is_sep = child_map < SP
    owner_id = jnp.where(is_sep, child_map // sep_dev, (child_map - SP) // bord_dev)
    target = jnp.where(is_sep, child_map % sep_dev, sep_dev + (child_map - SP) % bord_dev)
    slots = devices_all * capacity
    onehot = (owner_id[:, None] == jnp.arange(devices_all, dtype=jnp.int32)[None, :]).astype(
        jnp.int32
    )
    running = jnp.cumsum(onehot, axis=0)
    placed = owner_id * capacity + jnp.sum(onehot * running, axis=1) - 1
    spread = (jnp.arange(slots, dtype=jnp.int32)[:, None] == placed[None, :]).astype(jnp.float32)
    send_index = (
        jnp.full((slots,), sep_dev + bord_dev, jnp.int32).at[placed].set(target)
    )
    index_row = jnp.zeros((devices_all, 1, width_rhs), jnp.float32).at[:, 0, :capacity].set(
        send_index.reshape(devices_all, capacity).astype(jnp.float32)
    )
    send_rows = jnp.dot(spread, outgoing, precision=exact, preferred_element_type=jnp.float32)
    packed = jnp.concatenate(
        [send_rows.reshape(devices_all, capacity, width_rhs), index_row], axis=1
    )
    got = lax.all_to_all(packed, ALL, 0, 0, tiled=True)
    got_rows = got[:, :capacity].reshape(slots, width_rhs)
    got_index = got[:, capacity, :capacity].astype(jnp.int32).reshape(slots)
    gather_map = (
        jnp.arange(sep_dev + bord_dev, dtype=jnp.int32)[:, None] == got_index[None, :]
    ).astype(jnp.float32)
    received = jnp.dot(gather_map, got_rows, precision=exact, preferred_element_type=jnp.float32)
    sep_rows = parent_sep_rhs + received[:sep_dev]
    border_rows = parent_border_rhs + received[sep_dev:]
    partial_sep = lax.dot_general(
        parent_inverse,
        gather_chip(sep_rows, chips),
        contract_rows,
        precision=highest,
        preferred_element_type=jnp.float32,
    )
    parent_solution = gather(reduce_scatter(partial_sep, ROW, rows_axis), ROW, rows_axis)
    carried_parent = reduce_scatter_chip(parent_border, parent_solution, chips, highest)
    parent_contribution = border_rows - carried_parent
    return (child_part, parent_solution, parent_contribution)


def solution(mesh):
    rows, cols = mesh.devices.shape
    split = Mesh(mesh.devices.reshape(2, rows // 2, cols // 2, 2), ALL)
    placed = (
        P(ROW, COL),
        P(ROW, COL),
        P(ROW, None),
        P(ALL, None),
        P(ALL),
        P(ROW, COL),
        P(ROW, COL),
        P(ALL, None),
        P(ALL, None),
    )
    return jax.shard_map(
        local,
        mesh=split,
        in_specs=placed,
        out_specs=(P(COL, ROW), P(COL, None), P(ALL, None)),
        check_vma=False,
    )
```

```python
import jax
import jax.numpy as jnp
from jax import lax
from jax.sharding import Mesh
from jax.sharding import PartitionSpec as P

SP = 8192
ROW = ("h", "r8")
COL = ("x", "k")
ALL = ("h", "r8", "x", "k")


def reduce_scatter(x, axis, n):
    got = lax.all_to_all(x.reshape(n, x.shape[0] // n, x.shape[1]), axis, 0, 0, tiled=False)
    return got.sum(axis=0)


def reduce_scatter_chip(matrix, vector, chips, precision):
    first = lax.axis_index("k") == 0
    product = lax.dot_general(
        vector,
        matrix,
        (((0,), (1,)), ((), ())),
        precision=precision,
        preferred_element_type=jnp.float32,
    )
    blocks = product.reshape(product.shape[0], chips, 2, matrix.shape[0] // (2 * chips))
    even, odd = blocks[:, :, 0], blocks[:, :, 1]
    mine = jnp.where(first, even, odd)
    other = jnp.where(first, odd, even)
    summed = mine + lax.ppermute(other, "k", [(0, 1), (1, 0)])
    got = lax.all_to_all(summed, "x", 1, 1, tiled=False)
    return got.sum(axis=1).T


def gather(x, axis, n):
    got = lax.all_to_all(jnp.broadcast_to(x[None], (n,) + x.shape), axis, 0, 0, tiled=False)
    return got.reshape(n * x.shape[0], x.shape[1])


def local(
    child_inverse,
    child_border,
    child_sep_rhs,
    child_border_rhs,
    child_map,
    parent_inverse,
    parent_border,
    parent_sep_rhs,
    parent_border_rhs,
):
    highest = lax.Precision.HIGH
    exact = lax.Precision.HIGHEST
    contract_rows = (((0,), (0,)), ((), ()))
    half_rows = lax.axis_size("r8")
    rows_axis = lax.axis_size("h") * half_rows
    chips = lax.axis_size("x")
    cols_axis = chips * lax.axis_size("k")
    within = lax.axis_index("r8")
    partial_term = lax.dot_general(
        child_inverse,
        child_sep_rhs,
        contract_rows,
        precision=highest,
        preferred_element_type=jnp.float32,
    )
    width_rhs = partial_term.shape[1]
    solved = gather(reduce_scatter(partial_term, "r8", half_rows), "r8", half_rows)
    share = width_rhs // half_rows
    child_part = lax.dynamic_slice_in_dim(solved, within * share, share, axis=1)
    carried = reduce_scatter_chip(child_border, solved, chips, highest)
    outgoing = child_border_rhs - carried
    devices_all = rows_axis * cols_axis
    sep_dev = parent_sep_rhs.shape[0]
    bord_dev = parent_border_rhs.shape[0]
    rows_src = child_map.shape[0]
    capacity = rows_src // devices_all + 2
    is_sep = child_map < SP
    owner_id = jnp.where(is_sep, child_map // sep_dev, (child_map - SP) // bord_dev)
    target = jnp.where(is_sep, child_map % sep_dev, sep_dev + (child_map - SP) % bord_dev)
    slots = devices_all * capacity
    onehot = (owner_id[:, None] == jnp.arange(devices_all, dtype=jnp.int32)[None, :]).astype(
        jnp.int32
    )
    running = jnp.cumsum(onehot, axis=0)
    placed = owner_id * capacity + jnp.sum(onehot * running, axis=1) - 1
    spread = (jnp.arange(slots, dtype=jnp.int32)[:, None] == placed[None, :]).astype(jnp.float32)
    send_index = (
        jnp.full((slots,), sep_dev + bord_dev, jnp.int32).at[placed].set(target)
    )
    index_row = jnp.zeros((devices_all, 1, width_rhs), jnp.float32).at[:, 0, :capacity].set(
        send_index.reshape(devices_all, capacity).astype(jnp.float32)
    )
    send_rows = jnp.dot(spread, outgoing, precision=exact, preferred_element_type=jnp.float32)
    packed = jnp.concatenate(
        [send_rows.reshape(devices_all, capacity, width_rhs), index_row], axis=1
    )
    got = lax.all_to_all(packed, ALL, 0, 0, tiled=True)
    got_rows = got[:, :capacity].reshape(slots, width_rhs)
    got_index = got[:, capacity, :capacity].astype(jnp.int32).reshape(slots)
    gather_map = (
        jnp.arange(sep_dev + bord_dev, dtype=jnp.int32)[:, None] == got_index[None, :]
    ).astype(jnp.float32)
    received = jnp.dot(gather_map, got_rows, precision=exact, preferred_element_type=jnp.float32)
    sep_rows = parent_sep_rhs + received[:sep_dev]
    border_rows = parent_border_rhs + received[sep_dev:]
    partial_sep = lax.dot_general(
        parent_inverse,
        gather(sep_rows, COL, cols_axis),
        contract_rows,
        precision=highest,
        preferred_element_type=jnp.float32,
    )
    parent_solution = gather(reduce_scatter(partial_sep, ROW, rows_axis), ROW, rows_axis)
    carried_parent = reduce_scatter(
        jnp.dot(parent_border, parent_solution, precision=highest, preferred_element_type=jnp.float32),
        COL,
        cols_axis,
    )
    parent_contribution = border_rows - carried_parent
    return (child_part, parent_solution, parent_contribution)


def solution(mesh):
    rows, cols = mesh.devices.shape
    split = Mesh(mesh.devices.reshape(2, rows // 2, cols // 2, 2), ALL)
    placed = (
        P(ROW, COL),
        P(ROW, COL),
        P(ROW, None),
        P(ALL, None),
        P(ALL),
        P(ROW, COL),
        P(ROW, COL),
        P(ALL, None),
        P(ALL, None),
    )
    return jax.shard_map(
        local,
        mesh=split,
        in_specs=placed,
        out_specs=(P(COL, ROW), P(COL, None), P(ALL, None)),
        check_vma=False,
    )
```

```python
import jax
import jax.numpy as jnp
from jax import lax
from jax.sharding import Mesh
from jax.sharding import PartitionSpec as P

SP = 8192
ROW = ("h", "r8")
COL = ("x", "k")
ALL = ("h", "r8", "x", "k")


def reduce_scatter(x, axis, n):
    got = lax.all_to_all(x.reshape(n, x.shape[0] // n, x.shape[1]), axis, 0, 0, tiled=False)
    return got.sum(axis=0)


def reduce_scatter_cols(matrix, vector, n, precision):
    product = lax.dot_general(
        vector,
        matrix,
        (((0,), (1,)), ((), ())),
        precision=precision,
        preferred_element_type=jnp.float32,
    )
    blocks = product.reshape(product.shape[0], n, matrix.shape[0] // n)
    got = lax.all_to_all(blocks, COL, 1, 1, tiled=False)
    return got.sum(axis=1).T


def reduce_scatter_chip(matrix, vector, chips, precision):
    first = lax.axis_index("k") == 0
    product = lax.dot_general(
        vector,
        matrix,
        (((0,), (1,)), ((), ())),
        precision=precision,
        preferred_element_type=jnp.float32,
    )
    blocks = product.reshape(product.shape[0], chips, 2, matrix.shape[0] // (2 * chips))
    even, odd = blocks[:, :, 0], blocks[:, :, 1]
    mine = jnp.where(first, even, odd)
    other = jnp.where(first, odd, even)
    summed = mine + lax.ppermute(other, "k", [(0, 1), (1, 0)])
    got = lax.all_to_all(summed, "x", 1, 1, tiled=False)
    return got.sum(axis=1).T


def gather(x, axis, n):
    got = lax.all_to_all(jnp.broadcast_to(x[None], (n,) + x.shape), axis, 0, 0, tiled=False)
    return got.reshape(n * x.shape[0], x.shape[1])


def local(
    child_inverse,
    child_border,
    child_sep_rhs,
    child_border_rhs,
    child_map,
    parent_inverse,
    parent_border,
    parent_sep_rhs,
    parent_border_rhs,
):
    highest = lax.Precision.HIGH
    exact = lax.Precision.HIGHEST
    contract_rows = (((0,), (0,)), ((), ()))
    half_rows = lax.axis_size("r8")
    rows_axis = lax.axis_size("h") * half_rows
    chips = lax.axis_size("x")
    cols_axis = chips * lax.axis_size("k")
    within = lax.axis_index("r8")
    partial_term = lax.dot_general(
        child_inverse,
        child_sep_rhs,
        contract_rows,
        precision=highest,
        preferred_element_type=jnp.float32,
    )
    width_rhs = partial_term.shape[1]
    solved = gather(reduce_scatter(partial_term, "r8", half_rows), "r8", half_rows)
    share = width_rhs // half_rows
    child_part = lax.dynamic_slice_in_dim(solved, within * share, share, axis=1)
    carried = reduce_scatter_chip(child_border, solved, chips, highest)
    outgoing = child_border_rhs - carried
    devices_all = rows_axis * cols_axis
    sep_dev = parent_sep_rhs.shape[0]
    bord_dev = parent_border_rhs.shape[0]
    rows_src = child_map.shape[0]
    capacity = rows_src // devices_all + 2
    is_sep = child_map < SP
    owner_id = jnp.where(is_sep, child_map // sep_dev, (child_map - SP) // bord_dev)
    target = jnp.where(is_sep, child_map % sep_dev, sep_dev + (child_map - SP) % bord_dev)
    slots = devices_all * capacity
    onehot = (owner_id[:, None] == jnp.arange(devices_all, dtype=jnp.int32)[None, :]).astype(
        jnp.int32
    )
    running = jnp.cumsum(onehot, axis=0)
    placed = owner_id * capacity + jnp.sum(onehot * running, axis=1) - 1
    spread = (jnp.arange(slots, dtype=jnp.int32)[:, None] == placed[None, :]).astype(jnp.float32)
    send_index = (
        jnp.full((slots,), sep_dev + bord_dev, jnp.int32).at[placed].set(target)
    )
    index_row = jnp.zeros((devices_all, 1, width_rhs), jnp.float32).at[:, 0, :capacity].set(
        send_index.reshape(devices_all, capacity).astype(jnp.float32)
    )
    send_rows = jnp.dot(spread, outgoing, precision=exact, preferred_element_type=jnp.float32)
    packed = jnp.concatenate(
        [send_rows.reshape(devices_all, capacity, width_rhs), index_row], axis=1
    )
    got = lax.all_to_all(packed, ALL, 0, 0, tiled=True)
    got_rows = got[:, :capacity].reshape(slots, width_rhs)
    got_index = got[:, capacity, :capacity].astype(jnp.int32).reshape(slots)
    gather_map = (
        jnp.arange(sep_dev + bord_dev, dtype=jnp.int32)[:, None] == got_index[None, :]
    ).astype(jnp.float32)
    received = jnp.dot(gather_map, got_rows, precision=exact, preferred_element_type=jnp.float32)
    sep_rows = parent_sep_rhs + received[:sep_dev]
    border_rows = parent_border_rhs + received[sep_dev:]
    partial_sep = lax.dot_general(
        parent_inverse,
        gather(sep_rows, COL, cols_axis),
        contract_rows,
        precision=highest,
        preferred_element_type=jnp.float32,
    )
    parent_solution = gather(reduce_scatter(partial_sep, ROW, rows_axis), ROW, rows_axis)
    carried_parent = reduce_scatter_cols(parent_border, parent_solution, cols_axis, highest)
    parent_contribution = border_rows - carried_parent
    return (child_part, parent_solution, parent_contribution)


def solution(mesh):
    rows, cols = mesh.devices.shape
    split = Mesh(mesh.devices.reshape(2, rows // 2, cols // 2, 2), ALL)
    placed = (
        P(ROW, COL),
        P(ROW, COL),
        P(ROW, None),
        P(ALL, None),
        P(ALL),
        P(ROW, COL),
        P(ROW, COL),
        P(ALL, None),
        P(ALL, None),
    )
    return jax.shard_map(
        local,
        mesh=split,
        in_specs=placed,
        out_specs=(P(COL, ROW), P(COL, None), P(ALL, None)),
        check_vma=False,
    )
```

```python
import jax
import jax.numpy as jnp
from jax import lax
from jax.sharding import Mesh
from jax.sharding import PartitionSpec as P

SP = 8192
ROW = ("h", "r8")
COL = ("x", "k")
ALL = ("h", "r8", "x", "k")


def reduce_scatter(x, axis, n):
    got = lax.all_to_all(x.reshape(n, x.shape[0] // n, x.shape[1]), axis, 0, 0, tiled=False)
    return got.sum(axis=0)


def reduce_scatter_cols(matrix, vector, n, precision):
    product = lax.dot_general(
        vector,
        matrix,
        (((0,), (1,)), ((), ())),
        precision=precision,
        preferred_element_type=jnp.float32,
    )
    blocks = product.reshape(product.shape[0], n, matrix.shape[0] // n)
    got = lax.all_to_all(blocks, COL, 1, 1, tiled=False)
    return got.sum(axis=1).T


def reduce_scatter_chip(matrix, vector, chips, precision):
    first = lax.axis_index("k") == 0
    product = lax.dot_general(
        vector,
        matrix,
        (((0,), (1,)), ((), ())),
        precision=precision,
        preferred_element_type=jnp.float32,
    )
    blocks = product.reshape(product.shape[0], chips, 2, matrix.shape[0] // (2 * chips))
    even, odd = blocks[:, :, 0], blocks[:, :, 1]
    mine = jnp.where(first, even, odd)
    other = jnp.where(first, odd, even)
    summed = mine + lax.ppermute(other, "k", [(0, 1), (1, 0)])
    got = lax.all_to_all(summed, "x", 1, 1, tiled=False)
    return got.sum(axis=1).T


def gather(x, axis, n):
    got = lax.all_to_all(jnp.broadcast_to(x[None], (n,) + x.shape), axis, 0, 0, tiled=False)
    return got.reshape(n * x.shape[0], x.shape[1])


def local(
    child_inverse,
    child_border,
    child_sep_rhs,
    child_border_rhs,
    child_map,
    parent_inverse,
    parent_border,
    parent_sep_rhs,
    parent_border_rhs,
):
    highest = lax.Precision.HIGH
    exact = lax.Precision.HIGHEST
    contract_rows = (((0,), (0,)), ((), ()))
    half_rows = lax.axis_size("r8")
    rows_axis = lax.axis_size("h") * half_rows
    chips = lax.axis_size("x")
    cols_axis = chips * lax.axis_size("k")
    within = lax.axis_index("r8")
    partial_term = lax.dot_general(
        child_inverse,
        child_sep_rhs,
        contract_rows,
        precision=highest,
        preferred_element_type=jnp.float32,
    )
    width_rhs = partial_term.shape[1]
    solved = gather(reduce_scatter(partial_term, "r8", half_rows), "r8", half_rows)
    share = width_rhs // half_rows
    child_part = lax.dynamic_slice_in_dim(solved, within * share, share, axis=1)
    carried = reduce_scatter_chip(child_border, solved, chips, highest)
    outgoing = child_border_rhs - carried
    devices_all = rows_axis * cols_axis
    sep_dev = parent_sep_rhs.shape[0]
    bord_dev = parent_border_rhs.shape[0]
    rows_src = child_map.shape[0]
    capacity = rows_src // devices_all + 2
    is_sep = child_map < SP
    owner_id = jnp.where(is_sep, child_map // sep_dev, (child_map - SP) // bord_dev)
    target = jnp.where(is_sep, child_map % sep_dev, sep_dev + (child_map - SP) % bord_dev)
    slots = devices_all * capacity
    onehot = (owner_id[:, None] == jnp.arange(devices_all, dtype=jnp.int32)[None, :]).astype(
        jnp.int32
    )
    running = jnp.cumsum(onehot, axis=0)
    placed = owner_id * capacity + jnp.sum(onehot * running, axis=1) - 1
    spread = (jnp.arange(slots, dtype=jnp.int32)[:, None] == placed[None, :]).astype(jnp.float32)
    send_index = (
        jnp.full((slots,), sep_dev + bord_dev, jnp.int32).at[placed].set(target)
    )
    index_row = jnp.zeros((devices_all, 1, width_rhs), jnp.float32).at[:, 0, :capacity].set(
        send_index.reshape(devices_all, capacity).astype(jnp.float32)
    )
    send_rows = jnp.dot(spread, outgoing, precision=exact, preferred_element_type=jnp.float32)
    packed = jnp.concatenate(
        [send_rows.reshape(devices_all, capacity, width_rhs), index_row], axis=1
    )
    got = lax.all_to_all(packed, ALL, 0, 0, tiled=True)
    got_rows = got[:, :capacity].reshape(slots, width_rhs)
    got_index = got[:, capacity, :capacity].astype(jnp.int32).reshape(slots)
    gather_map = (
        jnp.arange(sep_dev + bord_dev, dtype=jnp.int32)[:, None] == got_index[None, :]
    ).astype(jnp.float32)
    received = jnp.dot(gather_map, got_rows, precision=exact, preferred_element_type=jnp.float32)
    sep_rows = parent_sep_rhs + received[:sep_dev]
    border_rows = parent_border_rhs + received[sep_dev:]
    partial_sep = lax.dot_general(
        parent_inverse,
        gather(sep_rows, COL, cols_axis),
        contract_rows,
        precision=highest,
        preferred_element_type=jnp.float32,
    )
    parent_solution = gather(reduce_scatter(partial_sep, ROW, rows_axis), ROW, rows_axis)
    carried_parent = reduce_scatter_chip(parent_border, parent_solution, chips, highest)
    parent_contribution = border_rows - carried_parent
    return (child_part, parent_solution, parent_contribution)


def solution(mesh):
    rows, cols = mesh.devices.shape
    split = Mesh(mesh.devices.reshape(2, rows // 2, cols // 2, 2), ALL)
    placed = (
        P(ROW, COL),
        P(ROW, COL),
        P(ROW, None),
        P(ALL, None),
        P(ALL),
        P(ROW, COL),
        P(ROW, COL),
        P(ALL, None),
        P(ALL, None),
    )
    return jax.shard_map(
        local,
        mesh=split,
        in_specs=placed,
        out_specs=(P(COL, ROW), P(COL, None), P(ALL, None)),
        check_vma=False,
    )
```

```python
import jax
import jax.numpy as jnp
from jax import lax
from jax.sharding import Mesh
from jax.sharding import PartitionSpec as P

SP = 8192
ROW = ("h", "r8")
COL = ("x", "k")
ALL = ("h", "r8", "x", "k")


def reduce_scatter(x, axis, n):
    got = lax.all_to_all(x.reshape(n, x.shape[0] // n, x.shape[1]), axis, 0, 0, tiled=False)
    return got.sum(axis=0)


def reduce_scatter_cols(matrix, vector, n, precision):
    product = lax.dot_general(
        vector,
        matrix,
        (((0,), (1,)), ((), ())),
        precision=precision,
        preferred_element_type=jnp.float32,
    )
    blocks = product.reshape(product.shape[0], n, matrix.shape[0] // n)
    got = lax.all_to_all(blocks, COL, 1, 1, tiled=False)
    return got.sum(axis=1).T


def reduce_scatter_blocks(matrix, pieces, chips, precision):
    first = lax.axis_index("k") == 0
    product = lax.dot_general(
        pieces,
        matrix.reshape(matrix.shape[0], pieces.shape[0], pieces.shape[1]),
        (((0, 1), (1, 2)), ((), ())),
        precision=precision,
        preferred_element_type=jnp.float32,
    )
    blocks = product.reshape(product.shape[0], chips, 2, matrix.shape[0] // (2 * chips))
    even, odd = blocks[:, :, 0], blocks[:, :, 1]
    mine = jnp.where(first, even, odd)
    other = jnp.where(first, odd, even)
    summed = mine + lax.ppermute(other, "k", [(0, 1), (1, 0)])
    got = lax.all_to_all(summed, "x", 1, 1, tiled=False)
    return got.sum(axis=1).T


def reduce_scatter_chip(matrix, vector, chips, precision):
    first = lax.axis_index("k") == 0
    product = lax.dot_general(
        vector,
        matrix,
        (((0,), (1,)), ((), ())),
        precision=precision,
        preferred_element_type=jnp.float32,
    )
    blocks = product.reshape(product.shape[0], chips, 2, matrix.shape[0] // (2 * chips))
    even, odd = blocks[:, :, 0], blocks[:, :, 1]
    mine = jnp.where(first, even, odd)
    other = jnp.where(first, odd, even)
    summed = mine + lax.ppermute(other, "k", [(0, 1), (1, 0)])
    got = lax.all_to_all(summed, "x", 1, 1, tiled=False)
    return got.sum(axis=1).T


def gather(x, axis, n):
    got = lax.all_to_all(jnp.broadcast_to(x[None], (n,) + x.shape), axis, 0, 0, tiled=False)
    return got.reshape(n * x.shape[0], x.shape[1])


def local(
    child_inverse,
    child_border,
    child_sep_rhs,
    child_border_rhs,
    child_map,
    parent_inverse,
    parent_border,
    parent_sep_rhs,
    parent_border_rhs,
):
    highest = lax.Precision.HIGH
    exact = lax.Precision.HIGHEST
    contract_rows = (((0,), (0,)), ((), ()))
    half_rows = lax.axis_size("r8")
    rows_axis = lax.axis_size("h") * half_rows
    chips = lax.axis_size("x")
    cols_axis = chips * lax.axis_size("k")
    within = lax.axis_index("r8")
    partial_term = lax.dot_general(
        child_inverse,
        child_sep_rhs,
        contract_rows,
        precision=highest,
        preferred_element_type=jnp.float32,
    )
    width_rhs = partial_term.shape[1]
    pieces = lax.all_to_all(
        jnp.broadcast_to(
            reduce_scatter(partial_term, "r8", half_rows)[None],
            (half_rows, partial_term.shape[0] // half_rows, width_rhs),
        ),
        "r8",
        0,
        0,
        tiled=False,
    )
    solved = pieces.reshape(partial_term.shape)
    share = width_rhs // half_rows
    child_part = lax.dynamic_slice_in_dim(solved, within * share, share, axis=1)
    carried = reduce_scatter_blocks(child_border, pieces, chips, highest)
    outgoing = child_border_rhs - carried
    devices_all = rows_axis * cols_axis
    sep_dev = parent_sep_rhs.shape[0]
    bord_dev = parent_border_rhs.shape[0]
    rows_src = child_map.shape[0]
    capacity = rows_src // devices_all + 2
    is_sep = child_map < SP
    owner_id = jnp.where(is_sep, child_map // sep_dev, (child_map - SP) // bord_dev)
    target = jnp.where(is_sep, child_map % sep_dev, sep_dev + (child_map - SP) % bord_dev)
    slots = devices_all * capacity
    onehot = (owner_id[:, None] == jnp.arange(devices_all, dtype=jnp.int32)[None, :]).astype(
        jnp.int32
    )
    running = jnp.cumsum(onehot, axis=0)
    placed = owner_id * capacity + jnp.sum(onehot * running, axis=1) - 1
    spread = (jnp.arange(slots, dtype=jnp.int32)[:, None] == placed[None, :]).astype(jnp.float32)
    send_index = (
        jnp.full((slots,), sep_dev + bord_dev, jnp.int32).at[placed].set(target)
    )
    index_row = jnp.zeros((devices_all, 1, width_rhs), jnp.float32).at[:, 0, :capacity].set(
        send_index.reshape(devices_all, capacity).astype(jnp.float32)
    )
    send_rows = jnp.dot(spread, outgoing, precision=exact, preferred_element_type=jnp.float32)
    packed = jnp.concatenate(
        [send_rows.reshape(devices_all, capacity, width_rhs), index_row], axis=1
    )
    got = lax.all_to_all(packed, ALL, 0, 0, tiled=True)
    got_rows = got[:, :capacity].reshape(slots, width_rhs)
    got_index = got[:, capacity, :capacity].astype(jnp.int32).reshape(slots)
    gather_map = (
        jnp.arange(sep_dev + bord_dev, dtype=jnp.int32)[:, None] == got_index[None, :]
    ).astype(jnp.float32)
    received = jnp.dot(gather_map, got_rows, precision=exact, preferred_element_type=jnp.float32)
    sep_rows = parent_sep_rhs + received[:sep_dev]
    border_rows = parent_border_rhs + received[sep_dev:]
    partial_sep = lax.dot_general(
        parent_inverse,
        gather(sep_rows, COL, cols_axis),
        contract_rows,
        precision=highest,
        preferred_element_type=jnp.float32,
    )
    parent_solution = gather(reduce_scatter(partial_sep, ROW, rows_axis), ROW, rows_axis)
    carried_parent = reduce_scatter_chip(parent_border, parent_solution, chips, highest)
    parent_contribution = border_rows - carried_parent
    return (child_part, parent_solution, parent_contribution)


def solution(mesh):
    rows, cols = mesh.devices.shape
    split = Mesh(mesh.devices.reshape(2, rows // 2, cols // 2, 2), ALL)
    placed = (
        P(ROW, COL),
        P(ROW, COL),
        P(ROW, None),
        P(ALL, None),
        P(ALL),
        P(ROW, COL),
        P(ROW, COL),
        P(ALL, None),
        P(ALL, None),
    )
    return jax.shard_map(
        local,
        mesh=split,
        in_specs=placed,
        out_specs=(P(COL, ROW), P(COL, None), P(ALL, None)),
        check_vma=False,
    )
```

```python
import jax
import jax.numpy as jnp
from jax import lax
from jax.sharding import Mesh
from jax.sharding import PartitionSpec as P

SP = 8192
ROW = ("h", "r8")
COL = ("x", "k")
ALL = ("h", "r8", "x", "k")


def reduce_scatter(x, axis, n):
    got = lax.all_to_all(x.reshape(n, x.shape[0] // n, x.shape[1]), axis, 0, 0, tiled=False)
    return got.sum(axis=0)


def reduce_scatter_cols(matrix, vector, n, precision):
    product = lax.dot_general(
        vector,
        matrix,
        (((0,), (1,)), ((), ())),
        precision=precision,
        preferred_element_type=jnp.float32,
    )
    blocks = product.reshape(product.shape[0], n, matrix.shape[0] // n)
    got = lax.all_to_all(blocks, COL, 1, 1, tiled=False)
    return got.sum(axis=1).T


def reduce_scatter_chip(matrix, vector, chips, precision):
    first = lax.axis_index("k") == 0
    product = lax.dot_general(
        vector,
        matrix,
        (((0,), (1,)), ((), ())),
        precision=precision,
        preferred_element_type=jnp.float32,
    )
    blocks = product.reshape(product.shape[0], chips, 2, matrix.shape[0] // (2 * chips))
    even, odd = blocks[:, :, 0], blocks[:, :, 1]
    mine = jnp.where(first, even, odd)
    other = jnp.where(first, odd, even)
    summed = mine + lax.ppermute(other, "k", [(0, 1), (1, 0)])
    got = lax.all_to_all(summed, "x", 1, 1, tiled=False)
    return got.sum(axis=1).T


def gather(x, axis, n):
    got = lax.all_to_all(jnp.broadcast_to(x[None], (n,) + x.shape), axis, 0, 0, tiled=False)
    return got.reshape(n * x.shape[0], x.shape[1])


def local(
    child_inverse,
    child_border,
    child_sep_rhs,
    child_border_rhs,
    child_map,
    parent_inverse,
    parent_border,
    parent_sep_rhs,
    parent_border_rhs,
):
    highest = lax.Precision.HIGH
    exact = lax.Precision.HIGHEST
    contract_rows = (((0,), (0,)), ((), ()))
    half_rows = lax.axis_size("r8")
    rows_axis = lax.axis_size("h") * half_rows
    chips = lax.axis_size("x")
    cols_axis = chips * lax.axis_size("k")
    within = lax.axis_index("r8")
    partial_term = lax.dot_general(
        child_inverse,
        child_sep_rhs,
        contract_rows,
        precision=highest,
        preferred_element_type=jnp.float32,
    )
    width_rhs = partial_term.shape[1]
    solved = gather(reduce_scatter(partial_term, "r8", half_rows), "r8", half_rows)
    share = width_rhs // half_rows
    child_part = lax.dynamic_slice_in_dim(solved, within * share, share, axis=1)
    carried = reduce_scatter_chip(child_border, solved, chips, highest)
    outgoing = child_border_rhs - carried
    devices_all = rows_axis * cols_axis
    sep_dev = parent_sep_rhs.shape[0]
    bord_dev = parent_border_rhs.shape[0]
    rows_src = child_map.shape[0]
    capacity = rows_src // devices_all + 2
    is_sep = child_map < SP
    owner_id = jnp.where(is_sep, child_map // sep_dev, (child_map - SP) // bord_dev)
    target = jnp.where(is_sep, child_map % sep_dev, sep_dev + (child_map - SP) % bord_dev)
    slots = devices_all * capacity
    onehot = (owner_id[:, None] == jnp.arange(devices_all, dtype=jnp.int32)[None, :]).astype(
        jnp.int32
    )
    running = jnp.cumsum(onehot, axis=0)
    placed = owner_id * capacity + jnp.sum(onehot * running, axis=1) - 1
    spread = (jnp.arange(slots, dtype=jnp.int32)[:, None] == placed[None, :]).astype(jnp.float32)
    send_index = (
        jnp.full((slots,), sep_dev + bord_dev, jnp.int32).at[placed].set(target)
    )
    index_row = jnp.zeros((devices_all, capacity, width_rhs), jnp.float32).at[:, 0, :capacity].set(
        send_index.reshape(devices_all, capacity).astype(jnp.float32)
    )
    send_rows = jnp.dot(spread, outgoing, precision=exact, preferred_element_type=jnp.float32)
    packed = jnp.concatenate(
        [send_rows.reshape(devices_all, capacity, width_rhs), index_row], axis=1
    )
    got = lax.all_to_all(packed, ALL, 0, 0, tiled=True)
    got_rows = got[:, :capacity].reshape(slots, width_rhs)
    got_index = got[:, capacity, :capacity].astype(jnp.int32).reshape(slots)
    gather_map = (
        jnp.arange(sep_dev + bord_dev, dtype=jnp.int32)[:, None] == got_index[None, :]
    ).astype(jnp.float32)
    received = jnp.dot(gather_map, got_rows, precision=exact, preferred_element_type=jnp.float32)
    sep_rows = parent_sep_rhs + received[:sep_dev]
    border_rows = parent_border_rhs + received[sep_dev:]
    partial_sep = lax.dot_general(
        parent_inverse,
        gather(sep_rows, COL, cols_axis),
        contract_rows,
        precision=highest,
        preferred_element_type=jnp.float32,
    )
    parent_solution = gather(reduce_scatter(partial_sep, ROW, rows_axis), ROW, rows_axis)
    carried_parent = reduce_scatter_chip(parent_border, parent_solution, chips, highest)
    parent_contribution = border_rows - carried_parent
    return (child_part, parent_solution, parent_contribution)


def solution(mesh):
    rows, cols = mesh.devices.shape
    split = Mesh(mesh.devices.reshape(2, rows // 2, cols // 2, 2), ALL)
    placed = (
        P(ROW, COL),
        P(ROW, COL),
        P(ROW, None),
        P(ALL, None),
        P(ALL),
        P(ROW, COL),
        P(ROW, COL),
        P(ALL, None),
        P(ALL, None),
    )
    return jax.shard_map(
        local,
        mesh=split,
        in_specs=placed,
        out_specs=(P(COL, ROW), P(COL, None), P(ALL, None)),
        check_vma=False,
    )
```

```python
import jax
import jax.numpy as jnp
from jax import lax
from jax.sharding import Mesh
from jax.sharding import PartitionSpec as P

SP = 8192
ROW = ("h", "r8")
COL = ("x", "k")
ALL = ("h", "r8", "x", "k")


def reduce_scatter(x, axis, n):
    got = lax.all_to_all(x.reshape(n, x.shape[0] // n, x.shape[1]), axis, 0, 0, tiled=False)
    return got.sum(axis=0)


def reduce_scatter_cols(matrix, vector, n, precision):
    product = lax.dot_general(
        vector,
        matrix,
        (((0,), (1,)), ((), ())),
        precision=precision,
        preferred_element_type=jnp.float32,
    )
    blocks = product.reshape(product.shape[0], n, matrix.shape[0] // n)
    got = lax.all_to_all(blocks, COL, 1, 1, tiled=False)
    return got.sum(axis=1).T


def reduce_scatter_chip(matrix, vector, chips, precision):
    first = lax.axis_index("k") == 0
    product = lax.dot_general(
        vector,
        matrix,
        (((0,), (1,)), ((), ())),
        precision=precision,
        preferred_element_type=jnp.float32,
    )
    blocks = product.reshape(product.shape[0], chips, 2, matrix.shape[0] // (2 * chips))
    even, odd = blocks[:, :, 0], blocks[:, :, 1]
    mine = jnp.where(first, even, odd)
    other = jnp.where(first, odd, even)
    summed = mine + lax.ppermute(other, "k", [(0, 1), (1, 0)])
    got = lax.all_to_all(jnp.transpose(summed, (1, 2, 0)), "x", 0, 0, tiled=False)
    return got.sum(axis=0)


def gather(x, axis, n):
    got = lax.all_to_all(jnp.broadcast_to(x[None], (n,) + x.shape), axis, 0, 0, tiled=False)
    return got.reshape(n * x.shape[0], x.shape[1])


def local(
    child_inverse,
    child_border,
    child_sep_rhs,
    child_border_rhs,
    child_map,
    parent_inverse,
    parent_border,
    parent_sep_rhs,
    parent_border_rhs,
):
    highest = lax.Precision.HIGH
    exact = lax.Precision.HIGHEST
    contract_rows = (((0,), (0,)), ((), ()))
    half_rows = lax.axis_size("r8")
    rows_axis = lax.axis_size("h") * half_rows
    chips = lax.axis_size("x")
    cols_axis = chips * lax.axis_size("k")
    within = lax.axis_index("r8")
    partial_term = lax.dot_general(
        child_inverse,
        child_sep_rhs,
        contract_rows,
        precision=highest,
        preferred_element_type=jnp.float32,
    )
    width_rhs = partial_term.shape[1]
    solved = gather(reduce_scatter(partial_term, "r8", half_rows), "r8", half_rows)
    share = width_rhs // half_rows
    child_part = lax.dynamic_slice_in_dim(solved, within * share, share, axis=1)
    carried = reduce_scatter_chip(child_border, solved, chips, highest)
    outgoing = child_border_rhs - carried
    devices_all = rows_axis * cols_axis
    sep_dev = parent_sep_rhs.shape[0]
    bord_dev = parent_border_rhs.shape[0]
    rows_src = child_map.shape[0]
    capacity = rows_src // devices_all + 2
    is_sep = child_map < SP
    owner_id = jnp.where(is_sep, child_map // sep_dev, (child_map - SP) // bord_dev)
    target = jnp.where(is_sep, child_map % sep_dev, sep_dev + (child_map - SP) % bord_dev)
    slots = devices_all * capacity
    onehot = (owner_id[:, None] == jnp.arange(devices_all, dtype=jnp.int32)[None, :]).astype(
        jnp.int32
    )
    running = jnp.cumsum(onehot, axis=0)
    placed = owner_id * capacity + jnp.sum(onehot * running, axis=1) - 1
    spread = (jnp.arange(slots, dtype=jnp.int32)[:, None] == placed[None, :]).astype(jnp.float32)
    send_index = (
        jnp.full((slots,), sep_dev + bord_dev, jnp.int32).at[placed].set(target)
    )
    index_row = jnp.zeros((devices_all, capacity, width_rhs), jnp.float32).at[:, 0, :capacity].set(
        send_index.reshape(devices_all, capacity).astype(jnp.float32)
    )
    send_rows = jnp.dot(spread, outgoing, precision=exact, preferred_element_type=jnp.float32)
    packed = jnp.concatenate(
        [send_rows.reshape(devices_all, capacity, width_rhs), index_row], axis=1
    )
    got = lax.all_to_all(packed, ALL, 0, 0, tiled=True)
    got_rows = got[:, :capacity].reshape(slots, width_rhs)
    got_index = got[:, capacity, :capacity].astype(jnp.int32).reshape(slots)
    gather_map = (
        jnp.arange(sep_dev + bord_dev, dtype=jnp.int32)[:, None] == got_index[None, :]
    ).astype(jnp.float32)
    received = jnp.dot(gather_map, got_rows, precision=exact, preferred_element_type=jnp.float32)
    sep_rows = parent_sep_rhs + received[:sep_dev]
    border_rows = parent_border_rhs + received[sep_dev:]
    partial_sep = lax.dot_general(
        parent_inverse,
        gather(sep_rows, COL, cols_axis),
        contract_rows,
        precision=highest,
        preferred_element_type=jnp.float32,
    )
    parent_solution = gather(reduce_scatter(partial_sep, ROW, rows_axis), ROW, rows_axis)
    carried_parent = reduce_scatter_chip(parent_border, parent_solution, chips, highest)
    parent_contribution = border_rows - carried_parent
    return (child_part, parent_solution, parent_contribution)


def solution(mesh):
    rows, cols = mesh.devices.shape
    split = Mesh(mesh.devices.reshape(2, rows // 2, cols // 2, 2), ALL)
    placed = (
        P(ROW, COL),
        P(ROW, COL),
        P(ROW, None),
        P(ALL, None),
        P(ALL),
        P(ROW, COL),
        P(ROW, COL),
        P(ALL, None),
        P(ALL, None),
    )
    return jax.shard_map(
        local,
        mesh=split,
        in_specs=placed,
        out_specs=(P(COL, ROW), P(COL, None), P(ALL, None)),
        check_vma=False,
    )
```

```python
import jax
import jax.numpy as jnp
from jax import lax
from jax.sharding import Mesh
from jax.sharding import PartitionSpec as P

SP = 8192
ROW = ("h", "r8")
COL = ("x", "k")
ALL = ("h", "r8", "x", "k")


def reduce_scatter(x, axis, n):
    got = lax.all_to_all(x.reshape(n, x.shape[0] // n, x.shape[1]), axis, 0, 0, tiled=False)
    return got.sum(axis=0)


def reduce_scatter_cols(matrix, vector, n, precision):
    product = lax.dot_general(
        vector,
        matrix,
        (((0,), (1,)), ((), ())),
        precision=precision,
        preferred_element_type=jnp.float32,
    )
    blocks = product.reshape(product.shape[0], n, matrix.shape[0] // n)
    got = lax.all_to_all(blocks, COL, 1, 1, tiled=False)
    return got.sum(axis=1).T


def reduce_scatter_chip(matrix, vector, chips, precision):
    first = lax.axis_index("k") == 0
    product = lax.dot_general(
        vector,
        matrix,
        (((0,), (1,)), ((), ())),
        precision=precision,
        preferred_element_type=jnp.float32,
    )
    blocks = product.reshape(product.shape[0], chips, 2, matrix.shape[0] // (2 * chips))
    both = blocks + lax.ppermute(blocks, "k", [(0, 1), (1, 0)])
    summed = jnp.where(first, both[:, :, 0], both[:, :, 1])
    got = lax.all_to_all(jnp.transpose(summed, (1, 2, 0)), "x", 0, 0, tiled=False)
    return got.sum(axis=0)


def gather(x, axis, n):
    got = lax.all_to_all(jnp.broadcast_to(x[None], (n,) + x.shape), axis, 0, 0, tiled=False)
    return got.reshape(n * x.shape[0], x.shape[1])


def local(
    child_inverse,
    child_border,
    child_sep_rhs,
    child_border_rhs,
    child_map,
    parent_inverse,
    parent_border,
    parent_sep_rhs,
    parent_border_rhs,
):
    highest = lax.Precision.HIGH
    exact = lax.Precision.HIGHEST
    contract_rows = (((0,), (0,)), ((), ()))
    half_rows = lax.axis_size("r8")
    rows_axis = lax.axis_size("h") * half_rows
    chips = lax.axis_size("x")
    cols_axis = chips * lax.axis_size("k")
    within = lax.axis_index("r8")
    partial_term = lax.dot_general(
        child_inverse,
        child_sep_rhs,
        contract_rows,
        precision=highest,
        preferred_element_type=jnp.float32,
    )
    width_rhs = partial_term.shape[1]
    solved = gather(reduce_scatter(partial_term, "r8", half_rows), "r8", half_rows)
    share = width_rhs // half_rows
    child_part = lax.dynamic_slice_in_dim(solved, within * share, share, axis=1)
    carried = reduce_scatter_chip(child_border, solved, chips, highest)
    outgoing = child_border_rhs - carried
    devices_all = rows_axis * cols_axis
    sep_dev = parent_sep_rhs.shape[0]
    bord_dev = parent_border_rhs.shape[0]
    rows_src = child_map.shape[0]
    capacity = rows_src // devices_all + 2
    is_sep = child_map < SP
    owner_id = jnp.where(is_sep, child_map // sep_dev, (child_map - SP) // bord_dev)
    target = jnp.where(is_sep, child_map % sep_dev, sep_dev + (child_map - SP) % bord_dev)
    slots = devices_all * capacity
    onehot = (owner_id[:, None] == jnp.arange(devices_all, dtype=jnp.int32)[None, :]).astype(
        jnp.int32
    )
    running = jnp.cumsum(onehot, axis=0)
    placed = owner_id * capacity + jnp.sum(onehot * running, axis=1) - 1
    spread = (jnp.arange(slots, dtype=jnp.int32)[:, None] == placed[None, :]).astype(jnp.float32)
    send_index = (
        jnp.full((slots,), sep_dev + bord_dev, jnp.int32).at[placed].set(target)
    )
    index_row = jnp.zeros((devices_all, capacity, width_rhs), jnp.float32).at[:, 0, :capacity].set(
        send_index.reshape(devices_all, capacity).astype(jnp.float32)
    )
    send_rows = jnp.dot(spread, outgoing, precision=exact, preferred_element_type=jnp.float32)
    packed = jnp.concatenate(
        [send_rows.reshape(devices_all, capacity, width_rhs), index_row], axis=1
    )
    got = lax.all_to_all(packed, ALL, 0, 0, tiled=True)
    got_rows = got[:, :capacity].reshape(slots, width_rhs)
    got_index = got[:, capacity, :capacity].astype(jnp.int32).reshape(slots)
    gather_map = (
        jnp.arange(sep_dev + bord_dev, dtype=jnp.int32)[:, None] == got_index[None, :]
    ).astype(jnp.float32)
    received = jnp.dot(gather_map, got_rows, precision=exact, preferred_element_type=jnp.float32)
    sep_rows = parent_sep_rhs + received[:sep_dev]
    border_rows = parent_border_rhs + received[sep_dev:]
    partial_sep = lax.dot_general(
        parent_inverse,
        gather(sep_rows, COL, cols_axis),
        contract_rows,
        precision=highest,
        preferred_element_type=jnp.float32,
    )
    parent_solution = gather(reduce_scatter(partial_sep, ROW, rows_axis), ROW, rows_axis)
    carried_parent = reduce_scatter_chip(parent_border, parent_solution, chips, highest)
    parent_contribution = border_rows - carried_parent
    return (child_part, parent_solution, parent_contribution)


def solution(mesh):
    rows, cols = mesh.devices.shape
    split = Mesh(mesh.devices.reshape(2, rows // 2, cols // 2, 2), ALL)
    placed = (
        P(ROW, COL),
        P(ROW, COL),
        P(ROW, None),
        P(ALL, None),
        P(ALL),
        P(ROW, COL),
        P(ROW, COL),
        P(ALL, None),
        P(ALL, None),
    )
    return jax.shard_map(
        local,
        mesh=split,
        in_specs=placed,
        out_specs=(P(COL, ROW), P(COL, None), P(ALL, None)),
        check_vma=False,
    )
```
